256 devices in a mesh: grp: 16 (over y, x_lo, core), tm: 16 (over z, x_hi).
Axes of the slice: x: 4 (x_hi: 2, x_lo: 2; x = x_hi * 2 + x_lo), y: 4, z: 8, core: 2. Of those that a mesh axis runs over, the one named last changes fastest.
Arguments:
- motion: bfloat16 [1024, 128, 1024], P(('grp', 'tm')), may hold values from -30 to 30
- modulation: float32 [6, 1024], replicated, may hold values from -1.25 to 1.25
- w_temporal_qkv: bfloat16 [1024, 3072], replicated, may hold values from -1 to 1
- w_temporal_out: bfloat16 [1024, 1024], replicated, may hold values from -0.1875 to 0.1875
- w_inter_qkv: bfloat16 [1024, 3072], P('tm'), may hold values from -1 to 1
- w_inter_out: bfloat16 [1024, 1024], P('tm'), may hold values from -0.1875 to 0.1875
- links: int32 [16, 4], replicated, may hold values from 0 to 1, as said below
Outputs:
- motion_out: bfloat16 [1024, 128, 1024], P(('grp', 'tm'))
The draws below stay inside these ranges and needn't reach their ends.
Inputs may be any that keep to these rules, and one draw needn't show every extreme that they name: Every group has between 1 and 4 links; one group has all of them and another exactly one.
All inputs are finite; a program needn't handle non-finite values.
Results may differ from the reference program's by a relative error of at most 0.008.
Values may be sent and summed in bfloat16 or wider, within the bound.
No kernel may reach another device: no remote copies, remote signals or barrier semaphores. Data moves between devices by JAX's collectives and lax.ppermute only.
A program may use at most 128 MiB of HBM per device.

```python
import jax
import jax.numpy as jnp
from jax import lax

D = 1024
HEADS = 16
HEAD = 64
CG = 64
REACH = 2
GROUPS = 16
CHARS = 1024
FRAMES = 128


def draw_links(key, part):
    first_key, second_key, third_key = jax.random.split(key, 3)
    width_links = 2 * REACH
    group_counts = jax.random.randint(first_key, (GROUPS,), 1, width_links + 1)
    full_group = jax.random.randint(second_key, (), 0, GROUPS)
    single_group = (full_group + 1) % GROUPS
    group_ids = jnp.arange(GROUPS, dtype=jnp.int32)
    group_counts = jnp.where(group_ids == full_group, width_links, group_counts)
    group_counts = jnp.where(group_ids == single_group, 1, group_counts)
    orders = jax.vmap(lambda row_key: jax.random.permutation(row_key, width_links))(jax.random.split(third_key, GROUPS))
    return (orders < group_counts[:, None]).astype(jnp.int32)


def drawn_weight(key, salt):
    weight_key = jax.random.fold_in(key, salt)
    values = jnp.clip(jax.random.normal(weight_key, (D, 3 * D), jnp.float32), -4.0, 4.0)
    return values * D ** (-0.5)


def draw_motion(key, part):
    noise_field = jnp.clip(jax.random.normal(jax.random.fold_in(key, 7011), (CHARS, FRAMES, D), jnp.float32), -6.0, 6.0)
    return noise_field.astype(jnp.bfloat16)


def draw_modulation(key, part):
    draw_key = jax.random.fold_in(key, 7021)
    table_rows = jnp.clip(0.5 * jax.random.normal(draw_key, (6, D), jnp.float32), -1.25, 1.25)
    return table_rows


def draw_w_temporal_qkv(key, part):
    base_weight = drawn_weight(key, 7031)
    return base_weight.astype(jnp.bfloat16)


def draw_w_inter_qkv(key, part):
    base_weight = drawn_weight(key, 7041)
    return base_weight.astype(jnp.bfloat16)


def steps_of(stream_key, shape, cuts, least, top_value):
    def one(position, shards_of):
        heights = jax.random.uniform(jax.random.fold_in(jax.random.fold_in(stream_key, 6), position), (shards_of,), jnp.float32, least / len(cuts), top_value / len(cuts))
        return jnp.repeat(jnp.exp(heights), shape[position] // shards_of).reshape((-1,) + (1,) * (len(shape) - position - 1))

    factor_of = one(*cuts[0])
    for cut in cuts[1:]:
        factor_of = factor_of * one(*cut)
    return factor_of


def noise(key, shape, scale, bound, cuts=(), kind=jnp.bfloat16):
    result = scale * jax.random.normal(key, shape, jnp.float32)
    if cuts:
        result = result * steps_of(key, shape, cuts, -0.22, 0.18)
    return jnp.clip(result, -bound, bound).astype(kind)


def setup_inputs(seed: int = 0) -> dict:
    key_of = jax.random.split(jax.random.key(seed), 8)
    motion = draw_motion(jax.random.fold_in(key_of[7], 71), 0)
    modulation = draw_modulation(jax.random.fold_in(key_of[7], 71), 0)
    w_temporal_qkv = draw_w_temporal_qkv(jax.random.fold_in(key_of[7], 71), 0)
    w_temporal_out = noise(key_of[3], (D, D), D ** -0.5, 0.1875)
    w_inter_qkv = draw_w_inter_qkv(jax.random.fold_in(key_of[7], 71), 0)
    w_inter_out = noise(key_of[5], (D, D), D ** -0.5, 0.1875, ((0, 16),))
    links = draw_links(jax.random.fold_in(key_of[7], 71), 0)
    return {"motion": motion, "modulation": modulation, "w_temporal_qkv": w_temporal_qkv, "w_temporal_out": w_temporal_out, "w_inter_qkv": w_inter_qkv, "w_inter_out": w_inter_out, "links": links}


EPSILON = 1e-06

def modulate(field, modulation, first, second):
    values = field.astype(jnp.float32)
    mean_square = lax.optimization_barrier(jnp.mean(values * values, axis=-1, keepdims=True))
    scaled = values * lax.rsqrt(mean_square + EPSILON) * (1.0 + modulation[second]) + modulation[first]
    return scaled.astype(jnp.bfloat16)

def softmax_rows(scores):
    row_top = lax.optimization_barrier(jnp.max(scores, axis=-1, keepdims=True))
    weights = jnp.exp(scores - row_top)
    return (weights / lax.optimization_barrier(jnp.sum(weights, axis=-1, keepdims=True))).astype(jnp.bfloat16)

def first_half(block, modulation, w_temporal_qkv, w_temporal_out, w_inter_qkv):
    normed = modulate(block, modulation, 0, 1)
    packed = jnp.dot(normed.reshape(CG * FRAMES, D), w_temporal_qkv, preferred_element_type=jnp.float32)
    packed = packed.astype(jnp.bfloat16).reshape(CG, FRAMES, 3, HEADS, HEAD)
    queries = packed[:, :, 0].astype(jnp.float32)
    key_part = packed[:, :, 1].astype(jnp.float32)
    value_part = packed[:, :, 2].astype(jnp.float32)
    scores = jnp.einsum('nfhd,nghd->nhfg', queries, key_part) * HEAD ** (-0.5)
    weights = softmax_rows(scores).astype(jnp.float32)
    mixed_heads = jnp.einsum('nhfg,nghd->nfhd', weights, value_part).astype(jnp.bfloat16)
    projected = jnp.dot(mixed_heads.reshape(CG * FRAMES, D), w_temporal_out, preferred_element_type=jnp.float32)
    middle = (block.astype(jnp.float32) + modulation[2] * projected.reshape(CG, FRAMES, D)).astype(jnp.bfloat16)
    normed_inter = modulate(middle, modulation, 3, 4)
    inter_packed = jnp.dot(normed_inter.reshape(CG * FRAMES, D), w_inter_qkv, preferred_element_type=jnp.float32)
    return (middle, inter_packed.astype(jnp.bfloat16).reshape(CG, FRAMES, 3 * D))

def reference(motion, modulation, w_temporal_qkv, w_temporal_out, w_inter_qkv, w_inter_out, links):
    blocks = motion.reshape(GROUPS, CG, FRAMES, D)
    middles, packs = lax.map(lambda block: first_half(block, modulation, w_temporal_qkv, w_temporal_out, w_inter_qkv), blocks)
    offsets = [j + 1 for j in range(REACH)] + [REACH - 1 - j for j in range(REACH, 2 * REACH)]

    def second_half(index):
        packed = packs[index]
        rows = [packed[:, :, D:]]
        for offset in offsets:
            other = ((index + offset) % GROUPS).astype(jnp.int32)
            rows.append(packs[other][:, :, D:])
        stacked = jnp.concatenate(rows, axis=0)
        queries = packed[:, :, :D].reshape(CG, FRAMES, HEADS, HEAD).astype(jnp.float32)
        key_part = stacked[:, :, :D].reshape(-1, FRAMES, HEADS, HEAD).astype(jnp.float32)
        value_part = stacked[:, :, D:].reshape(-1, FRAMES, HEADS, HEAD).astype(jnp.float32)
        scores = jnp.einsum('cfhd,kfhd->fhck', queries, key_part) * HEAD ** (-0.5)
        allowed = jnp.concatenate([jnp.ones((1,), jnp.int32), links[index]])
        key_mask = jnp.repeat(allowed, CG) > 0
        scores = jnp.where(key_mask, scores, -jnp.inf)
        weights = softmax_rows(scores).astype(jnp.float32)
        mixed_heads = jnp.einsum('fhck,kfhd->cfhd', weights, value_part).astype(jnp.bfloat16)
        projected = jnp.dot(mixed_heads.reshape(CG * FRAMES, D), w_inter_out, preferred_element_type=jnp.float32)
        total = middles[index].astype(jnp.float32) + modulation[5] * projected.reshape(CG, FRAMES, D)
        return total.astype(jnp.bfloat16)
    outputs = lax.map(second_half, jnp.arange(GROUPS, dtype=jnp.int32))
    return outputs.reshape(CHARS, FRAMES, D)
```

```python
import jax
import jax.numpy as jnp
from jax import lax
from jax.sharding import PartitionSpec as P

HEAD = 64
REACH = 2


EPSILON = 1e-06


def from_group(block, axis, offset):
    count = lax.axis_size(axis)
    route = [((i + offset) % count, i) for i in range(count)]
    return lax.ppermute(block, axis, route)


def modulate(field, modulation, first, second):
    values = field.astype(jnp.float32)
    mean_square = jnp.mean(values * values, axis=-1, keepdims=True)
    scaled = (
        values * lax.rsqrt(mean_square + EPSILON) * (1.0 + modulation[second]) + modulation[first]
    )
    return scaled.astype(jnp.bfloat16)


def softmax_rows(scores):
    row_top = jnp.max(scores, axis=-1, keepdims=True)
    weights = jnp.exp(scores - row_top)
    return (weights / jnp.sum(weights, axis=-1, keepdims=True)).astype(jnp.bfloat16)


def gather_split_by_core(shard, axis_small, axis_pair):
    half = shard.shape[1] // 2
    pair_index = lax.axis_index(axis_pair) % 2
    mine = lax.dynamic_slice_in_dim(shard, pair_index * half, half, axis=1)
    gathered = lax.all_gather(mine, axis_small, axis=0, tiled=True)
    count = lax.axis_size(axis_pair)
    other = lax.ppermute(gathered, axis_pair, [(i, i ^ 1) for i in range(count)])
    return jnp.where(
        pair_index == 0,
        jnp.concatenate([gathered, other], axis=1),
        jnp.concatenate([other, gathered], axis=1),
    )


def per_device(motion, modulation, w_temporal_qkv, w_temporal_out, w_inter_qkv, w_inter_out, links):
    own_chars, all_frames, feature_width = motion.shape
    head_count = feature_width // HEAD
    scale = HEAD ** (-0.5)
    inter_qkv = gather_split_by_core(w_inter_qkv, "tm", "grp")
    inter_out = gather_split_by_core(w_inter_out, "tm", "grp")

    normed = modulate(motion, modulation, 0, 1)
    t_w = w_temporal_qkv.reshape(feature_width, 3, head_count, HEAD)
    t_packed = jnp.einsum(
        "nfk,kshd->snhfd", normed, t_w, preferred_element_type=jnp.float32
    ).astype(jnp.bfloat16)
    scores = jnp.einsum(
        "nhfd,nhgd->nhfg", t_packed[0], t_packed[1], preferred_element_type=jnp.float32
    ) * scale
    weights = softmax_rows(scores)
    t_mixed = jnp.einsum(
        "nhfg,nhgd->nhfd", weights, t_packed[2], preferred_element_type=jnp.float32
    ).astype(jnp.bfloat16)
    t_projected = jnp.einsum(
        "nhfd,hdo->nfo",
        t_mixed,
        w_temporal_out.reshape(head_count, HEAD, feature_width),
        preferred_element_type=jnp.float32,
    )
    middle = (motion.astype(jnp.float32) + modulation[2] * t_projected).astype(jnp.bfloat16)
    normed_inter = modulate(middle, modulation, 3, 4)

    frames_own = lax.all_to_all(normed_inter, "tm", split_axis=1, concat_axis=0, tiled=True)
    offsets = [j + 1 for j in range(REACH)] + [-(j + 1) for j in range(REACH)]
    others = [from_group(frames_own, "grp", offset) for offset in offsets]
    stacked = jnp.stack([frames_own] + others, axis=0)

    i_w = inter_qkv.reshape(feature_width, 3, head_count, HEAD)
    queries = jnp.einsum(
        "cfk,khd->fhcd", frames_own, i_w[:, 0], preferred_element_type=jnp.float32
    ).astype(jnp.bfloat16)
    pairs = jnp.einsum(
        "scfk,kthd->tfhscd", stacked, i_w[:, 1:], preferred_element_type=jnp.float32
    ).astype(jnp.bfloat16)
    scores = jnp.einsum(
        "fhcd,fhskd->fhcsk", queries, pairs[0], preferred_element_type=jnp.float32
    ) * scale
    own_links = lax.dynamic_index_in_dim(links, lax.axis_index("grp"), axis=0, keepdims=False)
    allowed = jnp.concatenate([jnp.ones((1,), jnp.int32), own_links]) > 0
    scores = jnp.where(allowed[:, None], scores, -jnp.inf)
    group_count, char_count = scores.shape[3], scores.shape[4]
    frame_count = scores.shape[0]
    weights = softmax_rows(
        scores.reshape(frame_count, head_count, char_count, group_count * char_count)
    ).reshape(scores.shape)
    mixed_heads = jnp.einsum(
        "fhcsk,fhskd->cfhd", weights, pairs[1], preferred_element_type=jnp.float32
    ).astype(jnp.bfloat16)
    mixed_chars = lax.all_to_all(
        mixed_heads.reshape(char_count, frame_count, feature_width),
        "tm",
        split_axis=0,
        concat_axis=1,
        tiled=True,
    )
    result = jnp.dot(
        mixed_chars.reshape(own_chars * all_frames, feature_width),
        inter_out,
        preferred_element_type=jnp.float32,
    )
    total = middle.astype(jnp.float32) + modulation[5] * result.reshape(
        own_chars, all_frames, feature_width
    )
    return total.astype(jnp.bfloat16)


def solution(mesh):
    placed = (P(("grp", "tm"), None, None), P(), P(), P(), P("tm", None), P("tm", None), P())
    return jax.shard_map(
        per_device,
        mesh=mesh,
        in_specs=placed,
        out_specs=P(("grp", "tm"), None, None),
        check_vma=False,
    )
```

```python
import jax
import jax.numpy as jnp
from jax import lax
from jax.sharding import PartitionSpec as P

HEAD = 64
REACH = 2


EPSILON = 1e-06


def from_group(block, axis, offset):
    count = lax.axis_size(axis)
    route = [((i + offset) % count, i) for i in range(count)]
    return lax.ppermute(block, axis, route)


def modulate(field, modulation, first, second):
    values = field.astype(jnp.float32)
    mean_square = jnp.mean(values * values, axis=-1, keepdims=True)
    scaled = (
        values * lax.rsqrt(mean_square + EPSILON) * (1.0 + modulation[second]) + modulation[first]
    )
    return scaled.astype(jnp.bfloat16)


def softmax_rows(scores):
    row_top = jnp.max(scores, axis=-1, keepdims=True)
    weights = jnp.exp(scores - row_top)
    return (weights / jnp.sum(weights, axis=-1, keepdims=True)).astype(jnp.bfloat16)


def gather_split_by_core(shards, axis_small, axis_pair):
    pair_index = lax.axis_index(axis_pair) % 2
    halves = [shard.shape[1] // 2 for shard in shards]
    mine = jnp.concatenate(
        [
            lax.dynamic_slice_in_dim(shard, pair_index * half, half, axis=1)
            for shard, half in zip(shards, halves)
        ],
        axis=1,
    )
    gathered = lax.all_gather(mine, axis_small, axis=0, tiled=True)
    count = lax.axis_size(axis_pair)
    other = lax.ppermute(gathered, axis_pair, [(i, i ^ 1) for i in range(count)])
    results = []
    start = 0
    for half in halves:
        own_part = gathered[:, start:start + half]
        other_part = other[:, start:start + half]
        start += half
        results.append(
            jnp.where(
                pair_index == 0,
                jnp.concatenate([own_part, other_part], axis=1),
                jnp.concatenate([other_part, own_part], axis=1),
            )
        )
    return results


def per_device(motion, modulation, w_temporal_qkv, w_temporal_out, w_inter_qkv, w_inter_out, links):
    own_chars, all_frames, feature_width = motion.shape
    head_count = feature_width // HEAD
    scale = HEAD ** (-0.5)
    inter_qkv, inter_out = gather_split_by_core((w_inter_qkv, w_inter_out), "tm", "grp")

    normed = modulate(motion, modulation, 0, 1)
    t_w = w_temporal_qkv.reshape(feature_width, 3, head_count, HEAD)
    t_packed = jnp.einsum(
        "nfk,kshd->snhfd", normed, t_w, preferred_element_type=jnp.float32
    ).astype(jnp.bfloat16)
    scores = jnp.einsum(
        "nhfd,nhgd->nhfg", t_packed[0], t_packed[1], preferred_element_type=jnp.float32
    ) * scale
    weights = softmax_rows(scores)
    t_mixed = jnp.einsum(
        "nhfg,nhgd->nhfd", weights, t_packed[2], preferred_element_type=jnp.float32
    ).astype(jnp.bfloat16)
    t_projected = jnp.einsum(
        "nhfd,hdo->nfo",
        t_mixed,
        w_temporal_out.reshape(head_count, HEAD, feature_width),
        preferred_element_type=jnp.float32,
    )
    middle = (motion.astype(jnp.float32) + modulation[2] * t_projected).astype(jnp.bfloat16)
    normed_inter = modulate(middle, modulation, 3, 4)

    frames_own = lax.all_to_all(normed_inter, "tm", split_axis=1, concat_axis=0, tiled=True)
    offsets = [j + 1 for j in range(REACH)] + [-(j + 1) for j in range(REACH)]
    others = [from_group(frames_own, "grp", offset) for offset in offsets]
    stacked = jnp.concatenate([frames_own] + others, axis=0)
    char_count, frame_count, unused_width = frames_own.shape

    i_w = inter_qkv.reshape(feature_width, 3, head_count, HEAD)
    queries = jnp.einsum(
        "cfk,khd->fhcd", frames_own, i_w[:, 0], preferred_element_type=jnp.float32
    ).astype(jnp.bfloat16)
    pairs = jnp.einsum(
        "mfk,kthd->tfhmd", stacked, i_w[:, 1:], preferred_element_type=jnp.float32
    ).astype(jnp.bfloat16)
    scores = jnp.einsum(
        "fhcd,fhmd->fhcm", queries, pairs[0], preferred_element_type=jnp.float32
    ) * scale
    own_links = lax.dynamic_index_in_dim(links, lax.axis_index("grp"), axis=0, keepdims=False)
    allowed = jnp.concatenate([jnp.ones((1,), jnp.int32), own_links])
    key_mask = jnp.repeat(allowed, char_count) > 0
    scores = jnp.where(key_mask, scores, -jnp.inf)
    weights = softmax_rows(scores)
    mixed_heads = jnp.einsum(
        "fhcm,fhmd->cfhd", weights, pairs[1], preferred_element_type=jnp.float32
    ).astype(jnp.bfloat16)
    mixed_chars = lax.all_to_all(
        mixed_heads.reshape(char_count, frame_count, feature_width),
        "tm",
        split_axis=0,
        concat_axis=1,
        tiled=True,
    )
    result = jnp.dot(
        mixed_chars.reshape(own_chars * all_frames, feature_width),
        inter_out,
        preferred_element_type=jnp.float32,
    )
    total = middle.astype(jnp.float32) + modulation[5] * result.reshape(
        own_chars, all_frames, feature_width
    )
    return total.astype(jnp.bfloat16)


def solution(mesh):
    placed = (P(("grp", "tm"), None, None), P(), P(), P(), P("tm", None), P("tm", None), P())
    return jax.shard_map(
        per_device,
        mesh=mesh,
        in_specs=placed,
        out_specs=P(("grp", "tm"), None, None),
        check_vma=False,
    )
```

```python
import jax
import jax.numpy as jnp
from jax import lax
from jax.sharding import PartitionSpec as P

HEAD = 64
REACH = 2


EPSILON = 1e-06


def from_group(block, axis, offset):
    count = lax.axis_size(axis)
    route = [((i + offset) % count, i) for i in range(count)]
    return lax.ppermute(block, axis, route)


def modulate(field, modulation, first, second):
    values = field.astype(jnp.float32)
    mean_square = jnp.mean(values * values, axis=-1, keepdims=True)
    scaled = (
        values * lax.rsqrt(mean_square + EPSILON) * (1.0 + modulation[second]) + modulation[first]
    )
    return scaled.astype(jnp.bfloat16)


def softmax_rows(scores):
    row_top = jnp.max(scores, axis=-1, keepdims=True)
    weights = jnp.exp(scores - row_top)
    return (weights / jnp.sum(weights, axis=-1, keepdims=True)).astype(jnp.bfloat16)


def gather_half_by_core(shards, axis_small, axis_pair):
    pair_index = lax.axis_index(axis_pair) % 2
    halves = [shard.shape[1] // 2 for shard in shards]
    mine = jnp.concatenate(
        [
            lax.dynamic_slice_in_dim(shard, pair_index * half, half, axis=1)
            for shard, half in zip(shards, halves)
        ],
        axis=1,
    )
    return lax.all_gather(mine, axis_small, axis=0, tiled=True), halves


def swap_halves(gathered, halves, axis_pair):
    pair_index = lax.axis_index(axis_pair) % 2
    count = lax.axis_size(axis_pair)
    other = lax.ppermute(gathered, axis_pair, [(i, i ^ 1) for i in range(count)])
    results = []
    start = 0
    for half in halves:
        own_part = gathered[:, start:start + half]
        other_part = other[:, start:start + half]
        start += half
        results.append(
            jnp.where(
                pair_index == 0,
                jnp.concatenate([own_part, other_part], axis=1),
                jnp.concatenate([other_part, own_part], axis=1),
            )
        )
    return results


def per_device(motion, modulation, w_temporal_qkv, w_temporal_out, w_inter_qkv, w_inter_out, links):
    own_chars, all_frames, feature_width = motion.shape
    head_count = feature_width // HEAD
    scale = HEAD ** (-0.5)
    gathered, halves = gather_half_by_core((w_inter_qkv, w_inter_out), "tm", "grp")

    normed = modulate(motion, modulation, 0, 1)
    t_w = w_temporal_qkv.reshape(feature_width, 3, head_count, HEAD)
    t_packed = jnp.einsum(
        "nfk,kshd->snhfd", normed, t_w, preferred_element_type=jnp.float32
    ).astype(jnp.bfloat16)
    scores = jnp.einsum(
        "nhfd,nhgd->nhfg", t_packed[0], t_packed[1], preferred_element_type=jnp.float32
    ) * scale
    weights = softmax_rows(scores)
    t_mixed = jnp.einsum(
        "nhfg,nhgd->nhfd", weights, t_packed[2], preferred_element_type=jnp.float32
    ).astype(jnp.bfloat16)
    t_projected = jnp.einsum(
        "nhfd,hdo->nfo",
        t_mixed,
        w_temporal_out.reshape(head_count, HEAD, feature_width),
        preferred_element_type=jnp.float32,
    )
    middle = (motion.astype(jnp.float32) + modulation[2] * t_projected).astype(jnp.bfloat16)
    normed_inter = modulate(middle, modulation, 3, 4)

    frames_own = lax.all_to_all(normed_inter, "tm", split_axis=1, concat_axis=0, tiled=True)
    offsets = [j + 1 for j in range(REACH)] + [-(j + 1) for j in range(REACH)]
    others = [from_group(frames_own, "grp", offset) for offset in offsets]
    gathered, *others = lax.optimization_barrier((gathered, *others))
    inter_qkv, inter_out = swap_halves(gathered, halves, "grp")
    char_count, frame_count, unused_width = frames_own.shape

    i_w = inter_qkv.reshape(feature_width, 3, head_count, HEAD)
    queries = jnp.einsum(
        "cfk,khd->fhcd", frames_own, i_w[:, 0], preferred_element_type=jnp.float32
    ).astype(jnp.bfloat16)
    stacked = jnp.concatenate([frames_own] + others, axis=0)
    pairs = jnp.einsum(
        "mfk,kthd->tfhmd", stacked, i_w[:, 1:], preferred_element_type=jnp.float32
    ).astype(jnp.bfloat16)
    scores = jnp.einsum(
        "fhcd,fhmd->fhcm", queries, pairs[0], preferred_element_type=jnp.float32
    ) * scale
    own_links = lax.dynamic_index_in_dim(links, lax.axis_index("grp"), axis=0, keepdims=False)
    allowed = jnp.concatenate([jnp.ones((1,), jnp.int32), own_links])
    key_mask = jnp.repeat(allowed, char_count) > 0
    scores = jnp.where(key_mask, scores, -jnp.inf)
    weights = softmax_rows(scores)
    mixed_heads = jnp.einsum(
        "fhcm,fhmd->cfhd", weights, pairs[1], preferred_element_type=jnp.float32
    ).astype(jnp.bfloat16)
    mixed_chars = lax.all_to_all(
        mixed_heads.reshape(char_count, frame_count, feature_width),
        "tm",
        split_axis=0,
        concat_axis=1,
        tiled=True,
    )
    result = jnp.dot(
        mixed_chars.reshape(own_chars * all_frames, feature_width),
        inter_out,
        preferred_element_type=jnp.float32,
    )
    total = middle.astype(jnp.float32) + modulation[5] * result.reshape(
        own_chars, all_frames, feature_width
    )
    return total.astype(jnp.bfloat16)


def solution(mesh):
    placed = (P(("grp", "tm"), None, None), P(), P(), P(), P("tm", None), P("tm", None), P())
    return jax.shard_map(
        per_device,
        mesh=mesh,
        in_specs=placed,
        out_specs=P(("grp", "tm"), None, None),
        check_vma=False,
    )
```

```python
import jax
import jax.numpy as jnp
from jax import lax
from jax.sharding import PartitionSpec as P

HEAD = 64
REACH = 2


EPSILON = 1e-06


def from_group(block, axis, offset):
    count = lax.axis_size(axis)
    route = [((i + offset) % count, i) for i in range(count)]
    return lax.ppermute(block, axis, route)


def modulate(field, modulation, first, second):
    values = field.astype(jnp.float32)
    mean_square = jnp.mean(values * values, axis=-1, keepdims=True)
    scaled = (
        values * lax.rsqrt(mean_square + EPSILON) * (1.0 + modulation[second]) + modulation[first]
    )
    return scaled.astype(jnp.bfloat16)


def softmax_rows(scores):
    row_top = jnp.max(scores, axis=-1, keepdims=True)
    weights = jnp.exp(scores - row_top)
    return (weights / jnp.sum(weights, axis=-1, keepdims=True)).astype(jnp.bfloat16)


def gather_half_by_core(shards, axis_small, axis_pair):
    pair_index = lax.axis_index(axis_pair) % 2
    halves = [shard.shape[1] // 2 for shard in shards]
    mine = jnp.concatenate(
        [
            lax.dynamic_slice_in_dim(shard, pair_index * half, half, axis=1)
            for shard, half in zip(shards, halves)
        ],
        axis=1,
    )
    return lax.all_gather(mine, axis_small, axis=0, tiled=True), halves


def swap_halves(gathered, halves, axis_pair):
    pair_index = lax.axis_index(axis_pair) % 2
    count = lax.axis_size(axis_pair)
    other = lax.ppermute(gathered, axis_pair, [(i, i ^ 1) for i in range(count)])
    results = []
    start = 0
    for half in halves:
        own_part = gathered[:, start:start + half]
        other_part = other[:, start:start + half]
        start += half
        results.append(
            jnp.where(
                pair_index == 0,
                jnp.concatenate([own_part, other_part], axis=1),
                jnp.concatenate([other_part, own_part], axis=1),
            )
        )
    return results


def per_device(motion, modulation, w_temporal_qkv, w_temporal_out, w_inter_qkv, w_inter_out, links):
    own_chars, all_frames, feature_width = motion.shape
    head_count = feature_width // HEAD
    scale = HEAD ** (-0.5)
    gathered, halves = gather_half_by_core((w_inter_qkv, w_inter_out), "tm", "grp")

    normed = modulate(motion, modulation, 0, 1)
    t_w = w_temporal_qkv.reshape(feature_width, 3, head_count, HEAD)
    t_packed = jnp.einsum(
        "nfk,kshd->snhfd", normed, t_w, preferred_element_type=jnp.float32
    ).astype(jnp.bfloat16)
    scores = jnp.einsum(
        "nhfd,nhgd->nhfg", t_packed[0], t_packed[1], preferred_element_type=jnp.float32
    ) * scale
    weights = softmax_rows(scores)
    t_mixed = jnp.einsum(
        "nhfg,nhgd->nhfd", weights, t_packed[2], preferred_element_type=jnp.float32
    ).astype(jnp.bfloat16)
    t_projected = jnp.einsum(
        "nhfd,hdo->nfo",
        t_mixed,
        w_temporal_out.reshape(head_count, HEAD, feature_width),
        preferred_element_type=jnp.float32,
    )
    middle = (motion.astype(jnp.float32) + modulation[2] * t_projected).astype(jnp.bfloat16)
    normed_inter = modulate(middle, modulation, 3, 4)

    frames_own = lax.all_to_all(normed_inter, "tm", split_axis=1, concat_axis=0, tiled=True)
    pair_index = lax.axis_index("grp") % 2
    group_count = lax.axis_size("grp")
    pair_route = [(i, i ^ 1) for i in range(group_count)]
    ahead_two = from_group(frames_own, "grp", 2)
    behind_two = from_group(frames_own, "grp", -2)
    pair_own = lax.ppermute(frames_own, "grp", pair_route)
    gathered, ahead_two, behind_two = lax.optimization_barrier((gathered, ahead_two, behind_two))
    relayed = lax.ppermute(
        jnp.where(pair_index == 0, ahead_two, behind_two), "grp", pair_route
    )
    ahead_one = jnp.where(pair_index == 0, pair_own, relayed)
    behind_one = jnp.where(pair_index == 0, relayed, pair_own)
    others = [ahead_one, ahead_two, behind_one, behind_two]
    inter_qkv, inter_out = swap_halves(gathered, halves, "grp")
    char_count, frame_count, unused_width = frames_own.shape

    i_w = inter_qkv.reshape(feature_width, 3, head_count, HEAD)
    queries = jnp.einsum(
        "cfk,khd->fhcd", frames_own, i_w[:, 0], preferred_element_type=jnp.float32
    ).astype(jnp.bfloat16)
    stacked = jnp.concatenate([frames_own] + others, axis=0)
    pairs = jnp.einsum(
        "mfk,kthd->tfhmd", stacked, i_w[:, 1:], preferred_element_type=jnp.float32
    ).astype(jnp.bfloat16)
    scores = jnp.einsum(
        "fhcd,fhmd->fhcm", queries, pairs[0], preferred_element_type=jnp.float32
    ) * scale
    own_links = lax.dynamic_index_in_dim(links, lax.axis_index("grp"), axis=0, keepdims=False)
    allowed = jnp.concatenate([jnp.ones((1,), jnp.int32), own_links])
    key_mask = jnp.repeat(allowed, char_count) > 0
    scores = jnp.where(key_mask, scores, -jnp.inf)
    weights = softmax_rows(scores)
    mixed_heads = jnp.einsum(
        "fhcm,fhmd->cfhd", weights, pairs[1], preferred_element_type=jnp.float32
    ).astype(jnp.bfloat16)
    mixed_chars = lax.all_to_all(
        mixed_heads.reshape(char_count, frame_count, feature_width),
        "tm",
        split_axis=0,
        concat_axis=1,
        tiled=True,
    )
    result = jnp.dot(
        mixed_chars.reshape(own_chars * all_frames, feature_width),
        inter_out,
        preferred_element_type=jnp.float32,
    )
    total = middle.astype(jnp.float32) + modulation[5] * result.reshape(
        own_chars, all_frames, feature_width
    )
    return total.astype(jnp.bfloat16)


def solution(mesh):
    placed = (P(("grp", "tm"), None, None), P(), P(), P(), P("tm", None), P("tm", None), P())
    return jax.shard_map(
        per_device,
        mesh=mesh,
        in_specs=placed,
        out_specs=P(("grp", "tm"), None, None),
        check_vma=False,
    )
```

```python
import jax
import jax.numpy as jnp
from jax import lax
from jax.sharding import PartitionSpec as P

HEAD = 64
REACH = 2


EPSILON = 1e-06


def from_group(block, axis, offset):
    count = lax.axis_size(axis)
    route = [((i + offset) % count, i) for i in range(count)]
    return lax.ppermute(block, axis, route)


def modulate(field, modulation, first, second):
    values = field.astype(jnp.float32)
    mean_square = jnp.mean(values * values, axis=-1, keepdims=True)
    scaled = (
        values * lax.rsqrt(mean_square + EPSILON) * (1.0 + modulation[second]) + modulation[first]
    )
    return scaled.astype(jnp.bfloat16)


def softmax_rows(scores):
    row_top = jnp.max(scores, axis=-1, keepdims=True)
    weights = jnp.exp(scores - row_top)
    return (weights / jnp.sum(weights, axis=-1, keepdims=True)).astype(jnp.bfloat16)


def gather_half_by_core(shards, axis_small, axis_pair):
    pair_index = lax.axis_index(axis_pair) % 2
    halves = [shard.shape[1] // 2 for shard in shards]
    mine = jnp.concatenate(
        [
            lax.dynamic_slice_in_dim(shard, pair_index * half, half, axis=1)
            for shard, half in zip(shards, halves)
        ],
        axis=1,
    )
    return lax.all_gather(mine, axis_small, axis=0, tiled=True), halves


def swap_halves(gathered, halves, axis_pair):
    pair_index = lax.axis_index(axis_pair) % 2
    count = lax.axis_size(axis_pair)
    other = lax.ppermute(gathered, axis_pair, [(i, i ^ 1) for i in range(count)])
    results = []
    start = 0
    for half in halves:
        own_part = gathered[:, start:start + half]
        other_part = other[:, start:start + half]
        start += half
        results.append(
            jnp.where(
                pair_index == 0,
                jnp.concatenate([own_part, other_part], axis=1),
                jnp.concatenate([other_part, own_part], axis=1),
            )
        )
    return results


def per_device(motion, modulation, w_temporal_qkv, w_temporal_out, w_inter_qkv, w_inter_out, links):
    own_chars, all_frames, feature_width = motion.shape
    head_count = feature_width // HEAD
    scale = HEAD ** (-0.5)
    gathered, halves = gather_half_by_core((w_inter_qkv, w_inter_out), "tm", "grp")

    normed = modulate(motion, modulation, 0, 1)
    t_packed = jnp.dot(
        normed.reshape(own_chars * all_frames, feature_width),
        w_temporal_qkv,
        preferred_element_type=jnp.float32,
    ).astype(jnp.bfloat16)
    t_packed = t_packed.reshape(own_chars, all_frames, 3, head_count, HEAD).transpose(2, 0, 3, 1, 4)
    scores = jnp.einsum(
        "nhfd,nhgd->nhfg", t_packed[0], t_packed[1], preferred_element_type=jnp.float32
    ) * scale
    weights = softmax_rows(scores)
    t_mixed = jnp.einsum(
        "nhfg,nhgd->nhfd", weights, t_packed[2], preferred_element_type=jnp.float32
    ).astype(jnp.bfloat16)
    t_projected = jnp.einsum(
        "nhfd,hdo->nfo",
        t_mixed,
        w_temporal_out.reshape(head_count, HEAD, feature_width),
        preferred_element_type=jnp.float32,
    )
    middle = (motion.astype(jnp.float32) + modulation[2] * t_projected).astype(jnp.bfloat16)
    normed_inter = modulate(middle, modulation, 3, 4)

    frames_own = lax.all_to_all(normed_inter, "tm", split_axis=1, concat_axis=0, tiled=True)
    pair_index = lax.axis_index("grp") % 2
    group_count = lax.axis_size("grp")
    pair_route = [(i, i ^ 1) for i in range(group_count)]
    ahead_two = from_group(frames_own, "grp", 2)
    behind_two = from_group(frames_own, "grp", -2)
    pair_own = lax.ppermute(frames_own, "grp", pair_route)
    gathered, ahead_two, behind_two = lax.optimization_barrier((gathered, ahead_two, behind_two))
    relayed = lax.ppermute(
        jnp.where(pair_index == 0, ahead_two, behind_two), "grp", pair_route
    )
    ahead_one = jnp.where(pair_index == 0, pair_own, relayed)
    behind_one = jnp.where(pair_index == 0, relayed, pair_own)
    others = [ahead_one, ahead_two, behind_one, behind_two]
    inter_qkv, inter_out = swap_halves(gathered, halves, "grp")
    char_count, frame_count, unused_width = frames_own.shape

    queries = jnp.dot(
        frames_own.reshape(char_count * frame_count, feature_width),
        inter_qkv[:, :feature_width],
        preferred_element_type=jnp.float32,
    ).astype(jnp.bfloat16)
    queries = queries.reshape(char_count, frame_count, head_count, HEAD).transpose(1, 2, 0, 3)
    stacked = jnp.concatenate([frames_own] + others, axis=0)
    pairs = jnp.dot(
        stacked.reshape(-1, feature_width),
        inter_qkv[:, feature_width:],
        preferred_element_type=jnp.float32,
    ).astype(jnp.bfloat16)
    pairs = pairs.reshape(-1, frame_count, 2, head_count, HEAD).transpose(2, 1, 3, 0, 4)
    scores = jnp.einsum(
        "fhcd,fhmd->fhcm", queries, pairs[0], preferred_element_type=jnp.float32
    ) * scale
    own_links = lax.dynamic_index_in_dim(links, lax.axis_index("grp"), axis=0, keepdims=False)
    allowed = jnp.concatenate([jnp.ones((1,), jnp.int32), own_links])
    key_mask = jnp.repeat(allowed, char_count) > 0
    scores = jnp.where(key_mask, scores, -jnp.inf)
    weights = softmax_rows(scores)
    mixed_heads = jnp.einsum(
        "fhcm,fhmd->cfhd", weights, pairs[1], preferred_element_type=jnp.float32
    ).astype(jnp.bfloat16)
    mixed_chars = lax.all_to_all(
        mixed_heads.reshape(char_count, frame_count, feature_width),
        "tm",
        split_axis=0,
        concat_axis=1,
        tiled=True,
    )
    result = jnp.dot(
        mixed_chars.reshape(own_chars * all_frames, feature_width),
        inter_out,
        preferred_element_type=jnp.float32,
    )
    total = middle.astype(jnp.float32) + modulation[5] * result.reshape(
        own_chars, all_frames, feature_width
    )
    return total.astype(jnp.bfloat16)


def solution(mesh):
    placed = (P(("grp", "tm"), None, None), P(), P(), P(), P("tm", None), P("tm", None), P())
    return jax.shard_map(
        per_device,
        mesh=mesh,
        in_specs=placed,
        out_specs=P(("grp", "tm"), None, None),
        check_vma=False,
    )
```

```python
import jax
import jax.numpy as jnp
from jax import lax
from jax.sharding import PartitionSpec as P

HEAD = 64
REACH = 2


EPSILON = 1e-06


def from_group(block, axis, offset):
    count = lax.axis_size(axis)
    route = [((i + offset) % count, i) for i in range(count)]
    return lax.ppermute(block, axis, route)


def modulate(field, modulation, first, second):
    values = field.astype(jnp.float32)
    mean_square = jnp.mean(values * values, axis=-1, keepdims=True)
    scaled = (
        values * lax.rsqrt(mean_square + EPSILON) * (1.0 + modulation[second]) + modulation[first]
    )
    return scaled.astype(jnp.bfloat16)


def softmax_rows(scores):
    row_top = jnp.max(scores, axis=-1, keepdims=True)
    weights = jnp.exp(scores - row_top)
    return (weights / jnp.sum(weights, axis=-1, keepdims=True)).astype(jnp.bfloat16)


def gather_half_by_core(shards, axis_small, axis_pair):
    pair_index = lax.axis_index(axis_pair) % 2
    halves = [shard.shape[1] // 2 for shard in shards]
    mine = jnp.concatenate(
        [
            lax.dynamic_slice_in_dim(shard, pair_index * half, half, axis=1).T
            for shard, half in zip(shards, halves)
        ],
        axis=0,
    )
    return lax.all_gather(mine, axis_small, axis=1, tiled=True), halves


def swap_halves(gathered, halves, axis_pair):
    pair_index = lax.axis_index(axis_pair) % 2
    count = lax.axis_size(axis_pair)
    other = lax.ppermute(gathered, axis_pair, [(i, i ^ 1) for i in range(count)])
    results = []
    start = 0
    for half in halves:
        own_part = gathered[start:start + half]
        other_part = other[start:start + half]
        start += half
        results.append(
            jnp.where(
                pair_index == 0,
                jnp.concatenate([own_part, other_part], axis=0),
                jnp.concatenate([other_part, own_part], axis=0),
            )
        )
    return results


def per_device(motion, modulation, w_temporal_qkv, w_temporal_out, w_inter_qkv, w_inter_out, links):
    own_chars, all_frames, feature_width = motion.shape
    head_count = feature_width // HEAD
    scale = HEAD ** (-0.5)
    gathered, halves = gather_half_by_core((w_inter_qkv, w_inter_out), "tm", "grp")

    normed = modulate(motion, modulation, 0, 1)
    t_w = w_temporal_qkv.reshape(feature_width, 3, head_count, HEAD)
    t_packed = jnp.einsum(
        "nfk,kshd->snhfd", normed, t_w, preferred_element_type=jnp.float32
    ).astype(jnp.bfloat16)
    scores = jnp.einsum(
        "nhfd,nhgd->nhfg", t_packed[0], t_packed[1], preferred_element_type=jnp.float32
    ) * scale
    weights = softmax_rows(scores)
    t_mixed = jnp.einsum(
        "nhfg,nhgd->nhfd", weights, t_packed[2], preferred_element_type=jnp.float32
    ).astype(jnp.bfloat16)
    t_projected = jnp.einsum(
        "nhfd,hdo->nfo",
        t_mixed,
        w_temporal_out.reshape(head_count, HEAD, feature_width),
        preferred_element_type=jnp.float32,
    )
    middle = (motion.astype(jnp.float32) + modulation[2] * t_projected).astype(jnp.bfloat16)
    normed_inter = modulate(middle, modulation, 3, 4)

    frames_own = lax.all_to_all(normed_inter, "tm", split_axis=1, concat_axis=0, tiled=True)
    pair_index = lax.axis_index("grp") % 2
    group_count = lax.axis_size("grp")
    pair_route = [(i, i ^ 1) for i in range(group_count)]
    ahead_two = from_group(frames_own, "grp", 2)
    behind_two = from_group(frames_own, "grp", -2)
    pair_own = lax.ppermute(frames_own, "grp", pair_route)
    gathered, ahead_two, behind_two = lax.optimization_barrier((gathered, ahead_two, behind_two))
    relayed = lax.ppermute(
        jnp.where(pair_index == 0, ahead_two, behind_two), "grp", pair_route
    )
    ahead_one = jnp.where(pair_index == 0, pair_own, relayed)
    behind_one = jnp.where(pair_index == 0, relayed, pair_own)
    others = [ahead_one, ahead_two, behind_one, behind_two]
    inter_qkv, inter_out = swap_halves(gathered, halves, "grp")
    char_count, frame_count, unused_width = frames_own.shape

    i_w = inter_qkv.reshape(3, head_count, HEAD, feature_width)
    queries = jnp.einsum(
        "cfk,hdk->fhcd", frames_own, i_w[0], preferred_element_type=jnp.float32
    ).astype(jnp.bfloat16)
    stacked = jnp.concatenate([frames_own] + others, axis=0)
    pairs = jnp.einsum(
        "mfk,thdk->tfhmd", stacked, i_w[1:], preferred_element_type=jnp.float32
    ).astype(jnp.bfloat16)
    scores = jnp.einsum(
        "fhcd,fhmd->fhcm", queries, pairs[0], preferred_element_type=jnp.float32
    ) * scale
    own_links = lax.dynamic_index_in_dim(links, lax.axis_index("grp"), axis=0, keepdims=False)
    allowed = jnp.concatenate([jnp.ones((1,), jnp.int32), own_links])
    key_mask = jnp.repeat(allowed, char_count) > 0
    scores = jnp.where(key_mask, scores, -jnp.inf)
    weights = softmax_rows(scores)
    mixed_heads = jnp.einsum(
        "fhcm,fhmd->cfhd", weights, pairs[1], preferred_element_type=jnp.float32
    ).astype(jnp.bfloat16)
    mixed_chars = lax.all_to_all(
        mixed_heads.reshape(char_count, frame_count, feature_width),
        "tm",
        split_axis=0,
        concat_axis=1,
        tiled=True,
    )
    result = jnp.einsum(
        "tk,ok->to",
        mixed_chars.reshape(own_chars * all_frames, feature_width),
        inter_out,
        preferred_element_type=jnp.float32,
    )
    total = middle.astype(jnp.float32) + modulation[5] * result.reshape(
        own_chars, all_frames, feature_width
    )
    return total.astype(jnp.bfloat16)


def solution(mesh):
    placed = (P(("grp", "tm"), None, None), P(), P(), P(), P("tm", None), P("tm", None), P())
    return jax.shard_map(
        per_device,
        mesh=mesh,
        in_specs=placed,
        out_specs=P(("grp", "tm"), None, None),
        check_vma=False,
    )
```

```python
import jax
import jax.numpy as jnp
from jax import lax
from jax.sharding import PartitionSpec as P

HEAD = 64
REACH = 2


EPSILON = 1e-06


def from_group(block, axis, offset):
    count = lax.axis_size(axis)
    route = [((i + offset) % count, i) for i in range(count)]
    return lax.ppermute(block, axis, route)


def modulate(field, modulation, first, second):
    values = field.astype(jnp.float32)
    mean_square = jnp.mean(values * values, axis=-1, keepdims=True)
    scaled = (
        values * lax.rsqrt(mean_square + EPSILON) * (1.0 + modulation[second]) + modulation[first]
    )
    return scaled.astype(jnp.bfloat16)


def softmax_rows(scores):
    row_top = jnp.max(scores, axis=-1, keepdims=True)
    weights = jnp.exp(scores - row_top)
    return (weights / jnp.sum(weights, axis=-1, keepdims=True)).astype(jnp.bfloat16)


def gather_half_by_core(shards, axis_small, axis_pair):
    pair_index = lax.axis_index(axis_pair) % 2
    halves = [shard.shape[1] // 2 for shard in shards]
    mine = jnp.concatenate(
        [
            lax.dynamic_slice_in_dim(shard, pair_index * half, half, axis=1).T
            for shard, half in zip(shards, halves)
        ],
        axis=0,
    )
    return lax.all_gather(mine, axis_small, axis=1, tiled=True), halves


def swap_halves(gathered, halves, axis_pair):
    pair_index = lax.axis_index(axis_pair) % 2
    count = lax.axis_size(axis_pair)
    results = []
    start = 0
    for half in halves:
        own_part = gathered[start:start + half]
        other_part = lax.ppermute(own_part, axis_pair, [(i, i ^ 1) for i in range(count)])
        start += half
        results.append(
            jnp.where(
                pair_index == 0,
                jnp.concatenate([own_part, other_part], axis=0),
                jnp.concatenate([other_part, own_part], axis=0),
            )
        )
    return results


def per_device(motion, modulation, w_temporal_qkv, w_temporal_out, w_inter_qkv, w_inter_out, links):
    own_chars, all_frames, feature_width = motion.shape
    head_count = feature_width // HEAD
    scale = HEAD ** (-0.5)
    gathered, halves = gather_half_by_core((w_inter_qkv, w_inter_out), "tm", "grp")

    normed = modulate(motion, modulation, 0, 1)
    t_w = w_temporal_qkv.reshape(feature_width, 3, head_count, HEAD)
    t_packed = jnp.einsum(
        "nfk,kshd->snhfd", normed, t_w, preferred_element_type=jnp.float32
    ).astype(jnp.bfloat16)
    scores = jnp.einsum(
        "nhfd,nhgd->nhfg", t_packed[0], t_packed[1], preferred_element_type=jnp.float32
    ) * scale
    weights = softmax_rows(scores)
    t_mixed = jnp.einsum(
        "nhfg,nhgd->nhfd", weights, t_packed[2], preferred_element_type=jnp.float32
    ).astype(jnp.bfloat16)
    t_projected = jnp.einsum(
        "nhfd,hdo->nfo",
        t_mixed,
        w_temporal_out.reshape(head_count, HEAD, feature_width),
        preferred_element_type=jnp.float32,
    )
    middle = (motion.astype(jnp.float32) + modulation[2] * t_projected).astype(jnp.bfloat16)
    normed_inter = modulate(middle, modulation, 3, 4)

    frames_own = lax.all_to_all(normed_inter, "tm", split_axis=1, concat_axis=0, tiled=True)
    pair_index = lax.axis_index("grp") % 2
    group_count = lax.axis_size("grp")
    pair_route = [(i, i ^ 1) for i in range(group_count)]
    ahead_two = from_group(frames_own, "grp", 2)
    behind_two = from_group(frames_own, "grp", -2)
    pair_own = lax.ppermute(frames_own, "grp", pair_route)
    gathered, ahead_two, behind_two = lax.optimization_barrier((gathered, ahead_two, behind_two))
    relayed = lax.ppermute(
        jnp.where(pair_index == 0, ahead_two, behind_two), "grp", pair_route
    )
    ahead_one = jnp.where(pair_index == 0, pair_own, relayed)
    behind_one = jnp.where(pair_index == 0, relayed, pair_own)
    others = [ahead_one, ahead_two, behind_one, behind_two]
    inter_qkv, inter_out = swap_halves(gathered, halves, "grp")
    char_count, frame_count, unused_width = frames_own.shape

    i_w = inter_qkv.reshape(3, head_count, HEAD, feature_width)
    queries = jnp.einsum(
        "cfk,hdk->fhcd", frames_own, i_w[0], preferred_element_type=jnp.float32
    ).astype(jnp.bfloat16)
    stacked = jnp.concatenate([frames_own] + others, axis=0)
    pairs = jnp.einsum(
        "mfk,thdk->tfhmd", stacked, i_w[1:], preferred_element_type=jnp.float32
    ).astype(jnp.bfloat16)
    scores = jnp.einsum(
        "fhcd,fhmd->fhcm", queries, pairs[0], preferred_element_type=jnp.float32
    ) * scale
    own_links = lax.dynamic_index_in_dim(links, lax.axis_index("grp"), axis=0, keepdims=False)
    allowed = jnp.concatenate([jnp.ones((1,), jnp.int32), own_links])
    key_mask = jnp.repeat(allowed, char_count) > 0
    scores = jnp.where(key_mask, scores, -jnp.inf)
    weights = softmax_rows(scores)
    mixed_heads = jnp.einsum(
        "fhcm,fhmd->cfhd", weights, pairs[1], preferred_element_type=jnp.float32
    ).astype(jnp.bfloat16)
    mixed_chars = lax.all_to_all(
        mixed_heads.reshape(char_count, frame_count, feature_width),
        "tm",
        split_axis=0,
        concat_axis=1,
        tiled=True,
    )
    result = jnp.einsum(
        "tk,ok->to",
        mixed_chars.reshape(own_chars * all_frames, feature_width),
        inter_out,
        preferred_element_type=jnp.float32,
    )
    total = middle.astype(jnp.float32) + modulation[5] * result.reshape(
        own_chars, all_frames, feature_width
    )
    return total.astype(jnp.bfloat16)


def solution(mesh):
    placed = (P(("grp", "tm"), None, None), P(), P(), P(), P("tm", None), P("tm", None), P())
    return jax.shard_map(
        per_device,
        mesh=mesh,
        in_specs=placed,
        out_specs=P(("grp", "tm"), None, None),
        check_vma=False,
    )
```

```python
import jax
import jax.numpy as jnp
from jax import lax
from jax.sharding import PartitionSpec as P

HEAD = 64
REACH = 2


EPSILON = 1e-06


def from_group(block, axis, offset):
    count = lax.axis_size(axis)
    route = [((i + offset) % count, i) for i in range(count)]
    return lax.ppermute(block, axis, route)


def modulate(field, modulation, first, second):
    values = field.astype(jnp.float32)
    mean_square = jnp.mean(values * values, axis=-1, keepdims=True)
    scaled = (
        values * lax.rsqrt(mean_square + EPSILON) * (1.0 + modulation[second]) + modulation[first]
    )
    return scaled.astype(jnp.bfloat16)


def softmax_rows(scores):
    row_top = jnp.max(scores, axis=-1, keepdims=True)
    weights = jnp.exp(scores - row_top)
    return (weights / jnp.sum(weights, axis=-1, keepdims=True)).astype(jnp.bfloat16)


def gather_half_by_core(shards, axis_small, axis_pair):
    pair_index = lax.axis_index(axis_pair) % 2
    halves = [shard.shape[1] // 2 for shard in shards]
    mine = jnp.concatenate(
        [
            lax.dynamic_slice_in_dim(shard, pair_index * half, half, axis=1).T
            for shard, half in zip(shards, halves)
        ],
        axis=0,
    )
    return lax.all_gather(mine, axis_small, axis=1, tiled=True), halves


def swap_halves(gathered, halves, axis_pair):
    pair_index = lax.axis_index(axis_pair) % 2
    count = lax.axis_size(axis_pair)
    other = lax.ppermute(gathered, axis_pair, [(i, i ^ 1) for i in range(count)])
    results = []
    start = 0
    for half in halves:
        own_part = gathered[start:start + half]
        other_part = other[start:start + half]
        start += half
        results.append(
            jnp.where(
                pair_index == 0,
                jnp.concatenate([own_part, other_part], axis=0),
                jnp.concatenate([other_part, own_part], axis=0),
            )
        )
    return results


def per_device(motion, modulation, w_temporal_qkv, w_temporal_out, w_inter_qkv, w_inter_out, links):
    own_chars, all_frames, feature_width = motion.shape
    head_count = feature_width // HEAD
    scale = HEAD ** (-0.5)
    gathered, halves = gather_half_by_core((w_inter_qkv, w_inter_out), "tm", "grp")

    normed = modulate(motion, modulation, 0, 1)
    t_w = w_temporal_qkv.reshape(feature_width, 3, head_count, HEAD)
    t_packed = jnp.einsum(
        "nfk,kshd->snhfd", normed, t_w, preferred_element_type=jnp.float32
    ).astype(jnp.bfloat16)
    scores = jnp.einsum(
        "nhfd,nhgd->nhfg", t_packed[0], t_packed[1], preferred_element_type=jnp.float32
    ) * scale
    weights = softmax_rows(scores)
    t_mixed = jnp.einsum(
        "nhfg,nhgd->nhfd", weights, t_packed[2], preferred_element_type=jnp.float32
    ).astype(jnp.bfloat16)
    t_projected = jnp.einsum(
        "nhfd,hdo->nfo",
        t_mixed,
        w_temporal_out.reshape(head_count, HEAD, feature_width),
        preferred_element_type=jnp.float32,
    )
    middle = (motion.astype(jnp.float32) + modulation[2] * t_projected).astype(jnp.bfloat16)
    normed_inter = modulate(middle, modulation, 3, 4)

    frames_own = lax.all_to_all(normed_inter, "tm", split_axis=1, concat_axis=0, tiled=True)
    pair_index = lax.axis_index("grp") % 2
    group_count = lax.axis_size("grp")
    pair_route = [(i, i ^ 1) for i in range(group_count)]
    ahead_two = from_group(frames_own, "grp", 2)
    behind_two = from_group(frames_own, "grp", -2)
    pair_own = lax.ppermute(frames_own, "grp", pair_route)
    gathered, ahead_two, behind_two = lax.optimization_barrier((gathered, ahead_two, behind_two))
    relayed = lax.ppermute(
        jnp.where(pair_index == 0, ahead_two, behind_two), "grp", pair_route
    )
    ahead_one = jnp.where(pair_index == 0, pair_own, relayed)
    behind_one = jnp.where(pair_index == 0, relayed, pair_own)
    others = [ahead_one, ahead_two, behind_one, behind_two]
    inter_qkv, inter_out = swap_halves(gathered, halves, "grp")
    char_count, frame_count, unused_width = frames_own.shape

    i_w = inter_qkv.reshape(3, head_count, HEAD, feature_width)
    queries = jnp.einsum(
        "cfk,hdk->fhcd", frames_own, i_w[0], preferred_element_type=jnp.float32
    ).astype(jnp.bfloat16)
    stacked = jnp.concatenate([frames_own] + others, axis=0)
    pairs = [
        jnp.einsum(
            "mfk,hdk->fhmd", stacked, i_w[part], preferred_element_type=jnp.float32
        ).astype(jnp.bfloat16)
        for part in (1, 2)
    ]
    scores = jnp.einsum(
        "fhcd,fhmd->fhcm", queries, pairs[0], preferred_element_type=jnp.float32
    ) * scale
    own_links = lax.dynamic_index_in_dim(links, lax.axis_index("grp"), axis=0, keepdims=False)
    allowed = jnp.concatenate([jnp.ones((1,), jnp.int32), own_links])
    key_mask = jnp.repeat(allowed, char_count) > 0
    scores = jnp.where(key_mask, scores, -jnp.inf)
    weights = softmax_rows(scores)
    mixed_heads = jnp.einsum(
        "fhcm,fhmd->cfhd", weights, pairs[1], preferred_element_type=jnp.float32
    ).astype(jnp.bfloat16)
    mixed_chars = lax.all_to_all(
        mixed_heads.reshape(char_count, frame_count, feature_width),
        "tm",
        split_axis=0,
        concat_axis=1,
        tiled=True,
    )
    result = jnp.einsum(
        "tk,ok->to",
        mixed_chars.reshape(own_chars * all_frames, feature_width),
        inter_out,
        preferred_element_type=jnp.float32,
    )
    total = middle.astype(jnp.float32) + modulation[5] * result.reshape(
        own_chars, all_frames, feature_width
    )
    return total.astype(jnp.bfloat16)


def solution(mesh):
    placed = (P(("grp", "tm"), None, None), P(), P(), P(), P("tm", None), P("tm", None), P())
    return jax.shard_map(
        per_device,
        mesh=mesh,
        in_specs=placed,
        out_specs=P(("grp", "tm"), None, None),
        check_vma=False,
    )
```

```python
import jax
import jax.numpy as jnp
from jax import lax
from jax.sharding import PartitionSpec as P

HEAD = 64
REACH = 2


EPSILON = 1e-06


def from_group(block, axis, offset):
    count = lax.axis_size(axis)
    route = [((i + offset) % count, i) for i in range(count)]
    return lax.ppermute(block, axis, route)


def modulate(field, modulation, first, second):
    values = field.astype(jnp.float32)
    mean_square = jnp.mean(values * values, axis=-1, keepdims=True)
    scaled = (
        values * lax.rsqrt(mean_square + EPSILON) * (1.0 + modulation[second]) + modulation[first]
    )
    return scaled.astype(jnp.bfloat16)


def softmax_rows(scores):
    row_top = jnp.max(scores, axis=-1, keepdims=True)
    weights = jnp.exp(scores - row_top)
    return (weights / jnp.sum(weights, axis=-1, keepdims=True)).astype(jnp.bfloat16)


def gather_half_by_core(w_qkv, w_out, axis_small, axis_pair):
    pair_index = lax.axis_index(axis_pair) % 2
    width = w_out.shape[1]
    half = width // 2
    pieces = [
        lax.dynamic_slice_in_dim(w_qkv, part * width + pair_index * half, half, axis=1).T
        for part in range(3)
    ]
    pieces.append(lax.dynamic_slice_in_dim(w_out, pair_index * half, half, axis=1).T)
    return lax.all_gather(jnp.concatenate(pieces, axis=0), axis_small, axis=1, tiled=True)


def assemble_halves(gathered, axis_pair):
    pair_index = lax.axis_index(axis_pair) % 2
    count = lax.axis_size(axis_pair)
    other = lax.ppermute(gathered, axis_pair, [(i, i ^ 1) for i in range(count)])
    half = gathered.shape[0] // 4
    qkv = jnp.stack(
        [
            jnp.concatenate(
                [gathered[part * half:(part + 1) * half], other[part * half:(part + 1) * half]],
                axis=0,
            )
            for part in range(3)
        ],
        axis=0,
    )
    own_out = gathered[3 * half:]
    other_out = other[3 * half:]
    out = jnp.where(
        pair_index == 0,
        jnp.concatenate([own_out, other_out], axis=0),
        jnp.concatenate([other_out, own_out], axis=0),
    )
    return qkv, out


def per_device(motion, modulation, w_temporal_qkv, w_temporal_out, w_inter_qkv, w_inter_out, links):
    own_chars, all_frames, feature_width = motion.shape
    head_count = feature_width // HEAD
    scale = HEAD ** (-0.5)
    gathered = gather_half_by_core(w_inter_qkv, w_inter_out, "tm", "grp")

    normed = modulate(motion, modulation, 0, 1)
    t_w = w_temporal_qkv.reshape(feature_width, 3, head_count, HEAD)
    t_packed = jnp.einsum(
        "nfk,kshd->snhfd", normed, t_w, preferred_element_type=jnp.float32
    ).astype(jnp.bfloat16)
    scores = jnp.einsum(
        "nhfd,nhgd->nhfg", t_packed[0], t_packed[1], preferred_element_type=jnp.float32
    ) * scale
    weights = softmax_rows(scores)
    t_mixed = jnp.einsum(
        "nhfg,nhgd->nhfd", weights, t_packed[2], preferred_element_type=jnp.float32
    ).astype(jnp.bfloat16)
    t_projected = jnp.einsum(
        "nhfd,hdo->nfo",
        t_mixed,
        w_temporal_out.reshape(head_count, HEAD, feature_width),
        preferred_element_type=jnp.float32,
    )
    middle = (motion.astype(jnp.float32) + modulation[2] * t_projected).astype(jnp.bfloat16)
    normed_inter = modulate(middle, modulation, 3, 4)

    frames_own = lax.all_to_all(normed_inter, "tm", split_axis=1, concat_axis=0, tiled=True)
    pair_index = lax.axis_index("grp") % 2
    group_count = lax.axis_size("grp")
    pair_route = [(i, i ^ 1) for i in range(group_count)]
    ahead_two = from_group(frames_own, "grp", 2)
    behind_two = from_group(frames_own, "grp", -2)
    pair_own = lax.ppermute(frames_own, "grp", pair_route)
    gathered, ahead_two, behind_two = lax.optimization_barrier((gathered, ahead_two, behind_two))
    relayed = lax.ppermute(
        jnp.where(pair_index == 0, ahead_two, behind_two), "grp", pair_route
    )
    ahead_one = jnp.where(pair_index == 0, pair_own, relayed)
    behind_one = jnp.where(pair_index == 0, relayed, pair_own)
    others = [ahead_one, ahead_two, behind_one, behind_two]
    inter_qkv, inter_out = assemble_halves(gathered, "grp")
    char_count, frame_count, unused_width = frames_own.shape

    i_w = inter_qkv.reshape(3, head_count, HEAD, feature_width)
    queries = jnp.einsum(
        "cfk,hdk->fhcd", frames_own, i_w[0], preferred_element_type=jnp.float32
    ).astype(jnp.bfloat16)
    stacked = jnp.concatenate([frames_own] + others, axis=0)
    pairs = [
        jnp.einsum(
            "mfk,hdk->fhmd", stacked, i_w[part], preferred_element_type=jnp.float32
        ).astype(jnp.bfloat16)
        for part in (1, 2)
    ]
    scores = jnp.einsum(
        "fhcd,fhmd->fhcm", queries, pairs[0], preferred_element_type=jnp.float32
    ) * scale
    own_links = lax.dynamic_index_in_dim(links, lax.axis_index("grp"), axis=0, keepdims=False)
    allowed = jnp.concatenate([jnp.ones((1,), jnp.int32), own_links])
    key_mask = jnp.repeat(allowed, char_count) > 0
    scores = jnp.where(key_mask, scores, -jnp.inf)
    weights = softmax_rows(scores)
    mixed_heads = jnp.einsum(
        "fhcm,fhmd->cfhd", weights, pairs[1], preferred_element_type=jnp.float32
    ).astype(jnp.bfloat16)
    mixed_heads = jnp.where(
        pair_index == 0, mixed_heads, jnp.roll(mixed_heads, head_count // 2, axis=2)
    )
    mixed_chars = lax.all_to_all(
        mixed_heads.reshape(char_count, frame_count, feature_width),
        "tm",
        split_axis=0,
        concat_axis=1,
        tiled=True,
    )
    result = jnp.einsum(
        "tk,ok->to",
        mixed_chars.reshape(own_chars * all_frames, feature_width),
        inter_out,
        preferred_element_type=jnp.float32,
    )
    total = middle.astype(jnp.float32) + modulation[5] * result.reshape(
        own_chars, all_frames, feature_width
    )
    return total.astype(jnp.bfloat16)


def solution(mesh):
    placed = (P(("grp", "tm"), None, None), P(), P(), P(), P("tm", None), P("tm", None), P())
    return jax.shard_map(
        per_device,
        mesh=mesh,
        in_specs=placed,
        out_specs=P(("grp", "tm"), None, None),
        check_vma=False,
    )
```

```python
import jax
import jax.numpy as jnp
from jax import lax
from jax.sharding import PartitionSpec as P

HEAD = 64
REACH = 2


EPSILON = 1e-06


def from_group(block, axis, offset):
    count = lax.axis_size(axis)
    route = [((i + offset) % count, i) for i in range(count)]
    return lax.ppermute(block, axis, route)


def modulate(field, modulation, first, second):
    values = field.astype(jnp.float32)
    mean_square = jnp.mean(values * values, axis=-1, keepdims=True)
    scaled = (
        values * lax.rsqrt(mean_square + EPSILON) * (1.0 + modulation[second]) + modulation[first]
    )
    return scaled.astype(jnp.bfloat16)


def softmax_rows(scores):
    row_top = jnp.max(scores, axis=-1, keepdims=True)
    weights = jnp.exp(scores - row_top)
    return (weights / jnp.sum(weights, axis=-1, keepdims=True)).astype(jnp.bfloat16)


def gather_half_by_core(w_qkv, w_out, axis_small, axis_pair):
    pair_index = lax.axis_index(axis_pair) % 2
    width = w_out.shape[1]
    half = width // 2
    pieces = [
        lax.dynamic_slice_in_dim(w_qkv, part * width + pair_index * half, half, axis=1).T
        for part in range(3)
    ]
    pieces.append(lax.dynamic_slice_in_dim(w_out, pair_index * half, half, axis=1).T)
    return lax.all_gather(jnp.concatenate(pieces, axis=0), axis_small, axis=1, tiled=True)


def assemble_halves(gathered, axis_pair):
    pair_index = lax.axis_index(axis_pair) % 2
    count = lax.axis_size(axis_pair)
    other = lax.ppermute(gathered, axis_pair, [(i, i ^ 1) for i in range(count)])
    half = gathered.shape[0] // 4
    qkv = jnp.stack(
        [
            jnp.concatenate(
                [gathered[part * half:(part + 1) * half], other[part * half:(part + 1) * half]],
                axis=0,
            )
            for part in range(3)
        ],
        axis=0,
    )
    own_out = gathered[3 * half:]
    other_out = other[3 * half:]
    out = jnp.where(
        pair_index == 0,
        jnp.concatenate([own_out, other_out], axis=0),
        jnp.concatenate([other_out, own_out], axis=0),
    )
    return qkv, out


def per_device(motion, modulation, w_temporal_qkv, w_temporal_out, w_inter_qkv, w_inter_out, links):
    own_chars, all_frames, feature_width = motion.shape
    head_count = feature_width // HEAD
    scale = HEAD ** (-0.5)
    gathered = gather_half_by_core(w_inter_qkv, w_inter_out, "tm", "grp")

    normed = modulate(motion, modulation, 0, 1)
    t_w = w_temporal_qkv.reshape(feature_width, 3, head_count, HEAD)
    t_packed = jnp.einsum(
        "nfk,kshd->snhfd", normed, t_w, preferred_element_type=jnp.float32
    ).astype(jnp.bfloat16)
    scores = jnp.einsum(
        "nhfd,nhgd->nhfg", t_packed[0], t_packed[1], preferred_element_type=jnp.float32
    ) * scale
    weights = softmax_rows(scores)
    t_mixed = jnp.einsum(
        "nhfg,nhgd->nhfd", weights, t_packed[2], preferred_element_type=jnp.float32
    ).astype(jnp.bfloat16)
    t_projected = jnp.einsum(
        "nhfd,hdo->nfo",
        t_mixed,
        w_temporal_out.reshape(head_count, HEAD, feature_width),
        preferred_element_type=jnp.float32,
    )
    middle = (motion.astype(jnp.float32) + modulation[2] * t_projected).astype(jnp.bfloat16)
    normed_inter = modulate(middle, modulation, 3, 4)

    frames_own = lax.all_to_all(normed_inter, "tm", split_axis=1, concat_axis=0, tiled=True)
    pair_index = lax.axis_index("grp") % 2
    group_count = lax.axis_size("grp")
    pair_route = [(i, i ^ 1) for i in range(group_count)]
    ahead_two = from_group(frames_own, "grp", 2)
    behind_two = from_group(frames_own, "grp", -2)
    pair_own = lax.ppermute(frames_own, "grp", pair_route)
    gathered, ahead_two, behind_two, pair_own = lax.optimization_barrier(
        (gathered, ahead_two, behind_two, pair_own)
    )
    relayed = lax.ppermute(
        jnp.where(pair_index == 0, ahead_two, behind_two), "grp", pair_route
    )
    ahead_one = jnp.where(pair_index == 0, pair_own, relayed)
    behind_one = jnp.where(pair_index == 0, relayed, pair_own)
    others = [ahead_one, ahead_two, behind_one, behind_two]
    inter_qkv, inter_out = assemble_halves(gathered, "grp")
    char_count, frame_count, unused_width = frames_own.shape

    i_w = inter_qkv.reshape(3, head_count, HEAD, feature_width)
    queries = jnp.einsum(
        "cfk,hdk->fhcd", frames_own, i_w[0], preferred_element_type=jnp.float32
    ).astype(jnp.bfloat16)
    stacked = jnp.concatenate([frames_own] + others, axis=0)
    pairs = [
        jnp.einsum(
            "mfk,hdk->fhmd", stacked, i_w[part], preferred_element_type=jnp.float32
        ).astype(jnp.bfloat16)
        for part in (1, 2)
    ]
    scores = jnp.einsum(
        "fhcd,fhmd->fhcm", queries, pairs[0], preferred_element_type=jnp.float32
    ) * scale
    own_links = lax.dynamic_index_in_dim(links, lax.axis_index("grp"), axis=0, keepdims=False)
    allowed = jnp.concatenate([jnp.ones((1,), jnp.int32), own_links])
    key_mask = jnp.repeat(allowed, char_count) > 0
    scores = jnp.where(key_mask, scores, -jnp.inf)
    weights = softmax_rows(scores)
    mixed_heads = jnp.einsum(
        "fhcm,fhmd->cfhd", weights, pairs[1], preferred_element_type=jnp.float32
    ).astype(jnp.bfloat16)
    mixed_heads = jnp.where(
        pair_index == 0, mixed_heads, jnp.roll(mixed_heads, head_count // 2, axis=2)
    )
    mixed_chars = lax.all_to_all(
        mixed_heads.reshape(char_count, frame_count, feature_width),
        "tm",
        split_axis=0,
        concat_axis=1,
        tiled=True,
    )
    result = jnp.einsum(
        "tk,ok->to",
        mixed_chars.reshape(own_chars * all_frames, feature_width),
        inter_out,
        preferred_element_type=jnp.float32,
    )
    total = middle.astype(jnp.float32) + modulation[5] * result.reshape(
        own_chars, all_frames, feature_width
    )
    return total.astype(jnp.bfloat16)


def solution(mesh):
    placed = (P(("grp", "tm"), None, None), P(), P(), P(), P("tm", None), P("tm", None), P())
    return jax.shard_map(
        per_device,
        mesh=mesh,
        in_specs=placed,
        out_specs=P(("grp", "tm"), None, None),
        check_vma=False,
    )
```

```python
import jax
import jax.numpy as jnp
from jax import lax
from jax.sharding import PartitionSpec as P

HEAD = 64
REACH = 2


EPSILON = 1e-06


def from_group(block, axis, offset):
    count = lax.axis_size(axis)
    route = [((i + offset) % count, i) for i in range(count)]
    return lax.ppermute(block, axis, route)


def modulate(field, modulation, first, second):
    values = field.astype(jnp.float32)
    mean_square = jnp.mean(values * values, axis=-1, keepdims=True)
    scaled = (
        values * lax.rsqrt(mean_square + EPSILON) * (1.0 + modulation[second]) + modulation[first]
    )
    return scaled.astype(jnp.bfloat16)


def softmax_rows(scores):
    row_top = jnp.max(scores, axis=-1, keepdims=True)
    weights = jnp.exp(scores - row_top)
    return (weights / jnp.sum(weights, axis=-1, keepdims=True)).astype(jnp.bfloat16)


def gather_half_by_core(w_qkv, w_out, axis_small, axis_pair):
    pair_index = lax.axis_index(axis_pair) % 2
    width = w_out.shape[1]
    half = width // 2
    pieces = [
        lax.dynamic_slice_in_dim(w_qkv, part * width + pair_index * half, half, axis=1).T
        for part in range(3)
    ]
    pieces.append(lax.dynamic_slice_in_dim(w_out, pair_index * half, half, axis=1).T)
    return lax.all_gather(jnp.concatenate(pieces, axis=0), axis_small, axis=1, tiled=True)


def assemble_halves(gathered, axis_pair):
    pair_index = lax.axis_index(axis_pair) % 2
    count = lax.axis_size(axis_pair)
    other = lax.ppermute(gathered, axis_pair, [(i, i ^ 1) for i in range(count)])
    half = gathered.shape[0] // 4
    qkv = jnp.stack(
        [
            jnp.concatenate(
                [gathered[part * half:(part + 1) * half], other[part * half:(part + 1) * half]],
                axis=0,
            )
            for part in range(3)
        ],
        axis=0,
    )
    own_out = gathered[3 * half:]
    other_out = other[3 * half:]
    out = jnp.where(
        pair_index == 0,
        jnp.concatenate([own_out, other_out], axis=0),
        jnp.concatenate([other_out, own_out], axis=0),
    )
    return qkv, out


def per_device(motion, modulation, w_temporal_qkv, w_temporal_out, w_inter_qkv, w_inter_out, links):
    own_chars, all_frames, feature_width = motion.shape
    head_count = feature_width // HEAD
    scale = HEAD ** (-0.5)
    gathered = gather_half_by_core(w_inter_qkv, w_inter_out, "tm", "grp")

    normed = modulate(motion, modulation, 0, 1)
    t_w = w_temporal_qkv.reshape(feature_width, 3, head_count, HEAD)
    t_packed = jnp.einsum(
        "nfk,kshd->snhfd", normed, t_w, preferred_element_type=jnp.float32
    ).astype(jnp.bfloat16)
    scores = jnp.einsum(
        "nhfd,nhgd->nhfg", t_packed[0], t_packed[1], preferred_element_type=jnp.float32
    ) * scale
    weights = softmax_rows(scores)
    t_mixed = jnp.einsum(
        "nhfg,nhgd->nhfd", weights, t_packed[2], preferred_element_type=jnp.float32
    ).astype(jnp.bfloat16)
    t_projected = jnp.einsum(
        "nhfd,hdo->nfo",
        t_mixed,
        w_temporal_out.reshape(head_count, HEAD, feature_width),
        preferred_element_type=jnp.float32,
    )
    middle = (motion.astype(jnp.float32) + modulation[2] * t_projected).astype(jnp.bfloat16)
    normed_inter = modulate(middle, modulation, 3, 4)

    frames_own = lax.all_to_all(normed_inter, "tm", split_axis=1, concat_axis=0, tiled=True)
    pair_index = lax.axis_index("grp") % 2
    group_count = lax.axis_size("grp")
    pair_route = [(i, i ^ 1) for i in range(group_count)]
    ahead_two = from_group(frames_own, "grp", 2)
    behind_two = from_group(frames_own, "grp", -2)
    pair_own = lax.ppermute(frames_own, "grp", pair_route)
    gathered, ahead_two, behind_two, pair_own = lax.optimization_barrier(
        (gathered, ahead_two, behind_two, pair_own)
    )
    relayed = lax.ppermute(
        jnp.where(pair_index == 0, ahead_two, behind_two), "grp", pair_route
    )
    others = [pair_own, ahead_two, relayed, behind_two]
    inter_qkv, inter_out = assemble_halves(gathered, "grp")
    char_count, frame_count, unused_width = frames_own.shape

    i_w = inter_qkv.reshape(3, head_count, HEAD, feature_width)
    queries = jnp.einsum(
        "cfk,hdk->fhcd", frames_own, i_w[0], preferred_element_type=jnp.float32
    ).astype(jnp.bfloat16)
    stacked = jnp.concatenate([frames_own] + others, axis=0)
    pairs = [
        jnp.einsum(
            "mfk,hdk->fhmd", stacked, i_w[part], preferred_element_type=jnp.float32
        ).astype(jnp.bfloat16)
        for part in (1, 2)
    ]
    scores = jnp.einsum(
        "fhcd,fhmd->fhcm", queries, pairs[0], preferred_element_type=jnp.float32
    ) * scale
    own_links = lax.dynamic_index_in_dim(links, lax.axis_index("grp"), axis=0, keepdims=False)
    own_links = jnp.where(pair_index == 0, own_links, own_links[jnp.array([2, 1, 0, 3])])
    allowed = jnp.concatenate([jnp.ones((1,), jnp.int32), own_links])
    key_mask = jnp.repeat(allowed, char_count) > 0
    scores = jnp.where(key_mask, scores, -jnp.inf)
    weights = softmax_rows(scores)
    mixed_heads = jnp.einsum(
        "fhcm,fhmd->cfhd", weights, pairs[1], preferred_element_type=jnp.float32
    ).astype(jnp.bfloat16)
    mixed_heads = jnp.where(
        pair_index == 0, mixed_heads, jnp.roll(mixed_heads, head_count // 2, axis=2)
    )
    mixed_chars = lax.all_to_all(
        mixed_heads.reshape(char_count, frame_count, feature_width),
        "tm",
        split_axis=0,
        concat_axis=1,
        tiled=True,
    )
    result = jnp.einsum(
        "tk,ok->to",
        mixed_chars.reshape(own_chars * all_frames, feature_width),
        inter_out,
        preferred_element_type=jnp.float32,
    )
    total = middle.astype(jnp.float32) + modulation[5] * result.reshape(
        own_chars, all_frames, feature_width
    )
    return total.astype(jnp.bfloat16)


def solution(mesh):
    placed = (P(("grp", "tm"), None, None), P(), P(), P(), P("tm", None), P("tm", None), P())
    return jax.shard_map(
        per_device,
        mesh=mesh,
        in_specs=placed,
        out_specs=P(("grp", "tm"), None, None),
        check_vma=False,
    )
```
